128 devices in a mesh: replica: 8 (over z_lo, y), space: 16 (over z_hi, x, core).
Axes of the slice: x: 4, y: 4, z: 4 (z_hi: 2, z_lo: 2; z = z_hi * 2 + z_lo), core: 2. Of those that a mesh axis runs over, the one named last changes fastest.
Arguments:
- inputs: bfloat16 [8, 128, 512, 256], P('replica', 'space'), may hold values from -6 to 6
- cotangent: bfloat16 [8, 128, 512, 256], P('replica', 'space'), may hold values from -6 to 6
- land_mask: int32 [128, 512], P('space'), may hold values 0 or 1
- weights: float32 [8, 2, 2304, 256], P('replica', None, 'space'), may hold values from -0.125 to 0.125
- momentum: float32 [8, 2, 2304, 256], P('replica', None, 'space'), may hold values from -6 to 6
- step: int32 [1], replicated, may hold values from 0 to 63
Outputs:
- grad_input: bfloat16 [8, 128, 512, 256], P('replica', 'space')
- new_weights: float32 [8, 2, 2304, 256], P('replica', None, 'space')
- new_momentum: float32 [8, 2, 2304, 256], P('replica', None, 'space')
The draws below stay inside these ranges and needn't reach their ends.
All inputs are finite; a program needn't handle non-finite values. No bound on the sum of `land_mask` on one device may be relied on, other than what follows from the above.
Results may differ from the reference program's by a relative error of at most 0.012.
Values may be sent and summed in bfloat16 or wider, within the bound.
No kernel may reach another device: no remote copies, remote signals or barrier semaphores. Data moves between devices by JAX's collectives and lax.ppermute only.
A program may use at most 256 MiB of HBM per device.

```python
import math
import jax
import jax.numpy as jnp
from jax import lax

C = 256
COLS = 512
KC = 2304
ROWS = 128
REPLICAS = 8


def touch_ends(drawn, rng, low, high):
    index_at = [jax.random.randint(jax.random.fold_in(rng, axis), (), 0, length) for axis, length in enumerate(drawn.shape)]
    longest = drawn.shape.index(max(drawn.shape))
    neighbour = index_at[:longest] + [(index_at[longest] + 1) % drawn.shape[longest]] + index_at[longest + 1:]
    return drawn.at[tuple(index_at)].set(low).at[tuple(neighbour)].set(high)


def level_of(stream_key, shape, shards, least, top_value):
    factor_of = 1.0
    for dim, shards_of in shards:
        steps = jax.random.uniform(jax.random.fold_in(jax.random.fold_in(stream_key, 6), dim), (shards_of,), jnp.float32, least / len(shards), top_value / len(shards))
        factor_of = factor_of * jnp.repeat(jnp.exp(steps), shape[dim] // shards_of).reshape((-1,) + (1,) * (len(shape) - 1 - dim))
    return factor_of


def gaussian(rng, dims, scale, limit, cuts=(), kind=jnp.bfloat16):
    array = jax.random.normal(rng, dims, jnp.float32) * scale
    if len(cuts) > 0:
        array = level_of(rng, dims, cuts, -0.22, 0.18) * array
    return jnp.clip(array, min=-limit, max=limit).astype(kind)


def setup_inputs(seed: int = 0) -> dict:
    key_of = jax.random.split(jax.random.key(seed), 7)
    return {
        "inputs": gaussian(key_of[0], (REPLICAS, ROWS, COLS, C), 1.0, 6.0, ((0, 8), (1, 16))),
        "cotangent": gaussian(key_of[1], (REPLICAS, ROWS, COLS, C), 1.0, 6.0, ((0, 8), (1, 16))),
        "land_mask": touch_ends((jax.random.randint(key_of[2], (ROWS, COLS), 0, 3) < 2).astype(jnp.int32), jax.random.fold_in(key_of[2], 1), 0, 1),
        "weights": gaussian(key_of[3], (REPLICAS, 2, KC, C), KC ** -0.5, 0.125, ((0, 8), (2, 16)), jnp.float32),
        "momentum": gaussian(key_of[4], (REPLICAS, 2, KC, C), 1.0, 6.0, ((0, 8), (2, 16)), jnp.float32),
        "step": jax.random.randint(key_of[5], (1,), 0, 64).astype(jnp.int32),
    }


def shifted(field, down, right):
    row_count = field.shape[0]
    col_count = field.shape[1]
    padded = jnp.pad(field, ((1, 1), (1, 1), (0, 0)))
    return padded[1 + down:1 + down + row_count, 1 + right:1 + right + col_count]

def kernel_block(kernel, tap_row, tap_col):
    chan_count = kernel.shape[1]
    first_row = (3 * tap_row + tap_col) * chan_count
    return kernel[first_row:first_row + chan_count]

def conv_ahead(field, kernel):
    summed = jnp.zeros(field.shape[:2] + (kernel.shape[1],), jnp.float32)
    for tap_row in range(3):
        for tap_col in range(3):
            summed = summed + jnp.einsum('hwc,cd->hwd', shifted(field, tap_row - 1, tap_col - 1), kernel_block(kernel, tap_row, tap_col))
    return summed

def conv_behind(field, kernel):
    summed = jnp.zeros(field.shape, jnp.float32)
    for tap_row in range(3):
        for tap_col in range(3):
            summed = summed + jnp.einsum('hwd,cd->hwc', shifted(field, 1 - tap_row, 1 - tap_col), kernel_block(kernel, tap_row, tap_col))
    return summed

def kernel_grad(field, upstream):
    blocks = []
    for tap_row in range(3):
        for tap_col in range(3):
            blocks.append(jnp.einsum('hwc,hwd->cd', shifted(field, tap_row - 1, tap_col - 1), upstream))
    return jnp.concatenate(blocks, axis=0)

def silu_slope(preact):
    sigma = jax.nn.sigmoid(preact)
    return sigma * (1.0 + preact * (1.0 - sigma))

def reference(inputs, cotangent, land_mask, weights, momentum, step):
    mask_bf = land_mask.astype(jnp.bfloat16)
    scale = 1.0 / math.sqrt(ROWS * COLS)

    def one_replica(entries):
        field_in, upstream, kernels_f = entries
        masked = upstream * mask_bf[:, :, None]
        kernels = lax.optimization_barrier(kernels_f.astype(jnp.bfloat16)).astype(jnp.float32)
        field_f = field_in.astype(jnp.float32)
        masked_f = masked.astype(jnp.float32)
        preact = conv_ahead(field_f, kernels[0])
        hidden = lax.optimization_barrier(jax.nn.silu(preact).astype(jnp.bfloat16)).astype(jnp.float32)
        back_hidden = conv_behind(masked_f, kernels[1])
        back_pre = lax.optimization_barrier((back_hidden * silu_slope(preact)).astype(jnp.bfloat16)).astype(jnp.float32)
        grad_in = (conv_behind(back_pre, kernels[0]) + masked_f).astype(jnp.bfloat16)
        grads = jnp.stack([kernel_grad(field_f, back_pre), kernel_grad(hidden, masked_f)]) * scale
        return (grad_in, grads)
    grad_input, grads = lax.map(one_replica, (inputs, cotangent, weights))
    moment = 0.9 * momentum + grads
    updated = weights - 0.01 * moment
    levels = REPLICAS.bit_length() - 1
    distance = jnp.left_shift(jnp.int32(1), step[0] % levels)
    new_weights = 0.5 * (updated + jnp.roll(updated, distance, axis=0))
    new_momentum = 0.5 * (moment + jnp.roll(moment, distance, axis=0))
    return (grad_input, new_weights, new_momentum)
```

```python
from functools import partial
import math

import jax
import jax.numpy as jnp
from jax import lax
from jax.sharding import PartitionSpec as P


def extended_2(shard, sides, width):
    for axis, dim in sides:
        size, length = (lax.axis_size(axis), shard.shape[dim])
        up = [(i, (i + 1) % size) for i in range(size - 1)]
        down = [(j, i) for i, j in up]
        last = lax.slice_in_dim(shard, length - width, length, axis=dim)
        initial = lax.slice_in_dim(shard, 0, width, axis=dim)
        before = lax.ppermute(last, axis, up)
        after = lax.ppermute(initial, axis, down)
        shard = jnp.concatenate([before, shard, after], axis=dim)
    return shard


def as_sent(shard):

    def short(part):
        return part.astype(jnp.bfloat16) if part.dtype == jnp.float32 else part

    return jax.tree.map(short, shard)


def passed_along(shard, axis, by):
    length = lax.axis_size(axis)
    return lax.ppermute(shard, axis, [(i, (i + by) % length) for i in range(length)])


def conv_ahead(extended, kernel):
    chan_count = extended.shape[-1]
    taps = kernel.reshape(3, 3, chan_count, kernel.shape[1])
    return lax.conv_general_dilated(
        extended[None],
        taps,
        (1, 1),
        ((0, 0), (1, 1)),
        dimension_numbers=("NHWC", "HWIO", "NHWC"),
        preferred_element_type=jnp.float32,
    )[0]


def conv_behind(extended, kernel):
    chan_count = kernel.shape[0] // 9
    taps = jnp.flip(kernel.reshape(3, 3, chan_count, kernel.shape[1]), (0, 1))
    return lax.conv_general_dilated(
        extended[None],
        taps,
        (1, 1),
        ((0, 0), (1, 1)),
        dimension_numbers=("NHWC", "HWOI", "NHWC"),
        preferred_element_type=jnp.float32,
    )[0]


def kernel_grad(extended, upstream):
    grad = lax.conv_general_dilated(
        extended[None],
        upstream[None],
        (1, 1),
        ((0, 0), (1, 1)),
        dimension_numbers=("CHWN", "IHWO", "HWNC"),
        preferred_element_type=jnp.float32,
    )
    return grad.reshape(-1, grad.shape[-1])


def silu_slope(preact):
    sigma = jax.nn.sigmoid(preact)
    return sigma * (1.0 + preact * (1.0 - sigma))


def rim(stacked):
    return extended_2(stacked, (("space", 1),), 1)


def send_both(distance, stacked):
    return jax.tree.map(
        lambda part, own: part.astype(own.dtype),
        passed_along(as_sent(stacked), "replica", distance),
        stacked,
    )


def gossip(step, stacked, sender):
    levels = lax.axis_size("replica").bit_length() - 1
    received = lax.switch(
        step[0] % levels, [partial(sender, 1 << power) for power in range(levels)], stacked
    )
    return 0.5 * (stacked + received)


def shards(inputs, cotangent, land_mask, weights, momentum, step):
    row_count = inputs.shape[1]
    col_count = inputs.shape[2]
    space_count = lax.axis_size("space")
    masked = cotangent[0] * land_mask.astype(jnp.bfloat16)[:, :, None]
    kernels = lax.all_gather(weights.astype(jnp.bfloat16), "space", axis=2, tiled=True)
    kernel_first = kernels[0, 0]
    kernel_second = kernels[0, 1]
    paired = rim(jnp.stack([inputs[0], masked]))
    preact = conv_ahead(paired[0], kernel_first)
    hidden = jax.nn.silu(preact).astype(jnp.bfloat16)
    hidden_ext = rim(hidden[None])[0]
    back_mid = (conv_behind(paired[1], kernel_second) * silu_slope(preact)).astype(jnp.bfloat16)
    back_ext = rim(back_mid[None])[0]
    input_ext = paired[0]
    grad_input = (conv_behind(back_ext, kernel_first) + masked.astype(jnp.float32)).astype(
        jnp.bfloat16
    )[None]
    scale = 1.0 / math.sqrt(row_count * space_count * col_count)
    grad_second_full = kernel_grad(hidden_ext, masked) * scale
    grad_first_full = kernel_grad(input_ext, back_mid) * scale
    shares = lax.psum_scatter(
        jnp.stack([grad_first_full, grad_second_full])[None].astype(jnp.bfloat16),
        "space",
        scatter_dimension=2,
        tiled=True,
    ).astype(jnp.float32)
    moment = 0.9 * momentum + shares
    updated = weights - 0.01 * moment
    mixed = gossip(step, jnp.stack([updated, moment]), send_both)
    new_weights = mixed[0]
    new_momentum = mixed[1]
    return (grad_input, new_weights, new_momentum)


def solution(mesh):
    in_specs = (
        P("replica", "space", None, None),
        P("replica", "space", None, None),
        P("space", None),
        P("replica", None, "space", None),
        P("replica", None, "space", None),
        P(),
    )
    out_specs = (
        P("replica", "space", None, None),
        P("replica", None, "space", None),
        P("replica", None, "space", None),
    )
    return jax.shard_map(shards, mesh=mesh, in_specs=in_specs, out_specs=out_specs, check_vma=False)
```

```python
from functools import partial
import math

import jax
import jax.numpy as jnp
from jax import lax
from jax.sharding import PartitionSpec as P


def extended_2(shard, sides, width):
    for axis, dim in sides:
        size, length = (lax.axis_size(axis), shard.shape[dim])
        up = [(i, (i + 1) % size) for i in range(size - 1)]
        down = [(j, i) for i, j in up]
        last = lax.slice_in_dim(shard, length - width, length, axis=dim)
        initial = lax.slice_in_dim(shard, 0, width, axis=dim)
        before = lax.ppermute(last, axis, up)
        after = lax.ppermute(initial, axis, down)
        shard = jnp.concatenate([before, shard, after], axis=dim)
    return shard


def as_sent(shard):

    def short(part):
        return part.astype(jnp.bfloat16) if part.dtype == jnp.float32 else part

    return jax.tree.map(short, shard)


def passed_along(shard, axis, by):
    length = lax.axis_size(axis)
    return lax.ppermute(shard, axis, [(i, (i + by) % length) for i in range(length)])


def conv_ahead(extended, kernel):
    chan_count = extended.shape[-1]
    taps = kernel.reshape(3, 3, chan_count, kernel.shape[1])
    return lax.conv_general_dilated(
        extended[None],
        taps,
        (1, 1),
        ((0, 0), (1, 1)),
        dimension_numbers=("NHWC", "HWIO", "NHWC"),
        preferred_element_type=jnp.float32,
    )[0]


def conv_behind(extended, kernel):
    chan_count = kernel.shape[0] // 9
    taps = jnp.flip(kernel.reshape(3, 3, chan_count, kernel.shape[1]), (0, 1))
    return lax.conv_general_dilated(
        extended[None],
        taps,
        (1, 1),
        ((0, 0), (1, 1)),
        dimension_numbers=("NHWC", "HWOI", "NHWC"),
        preferred_element_type=jnp.float32,
    )[0]


def kernel_grad(extended, upstream):
    grad = lax.conv_general_dilated(
        extended[None],
        upstream[None],
        (1, 1),
        ((0, 0), (1, 1)),
        dimension_numbers=("CHWN", "IHWO", "HWNC"),
        preferred_element_type=jnp.float32,
    )
    return grad.reshape(-1, grad.shape[-1])


def kernel_grad_behind(extended_upstream, field):
    grad = lax.conv_general_dilated(
        extended_upstream[None],
        field[None],
        (1, 1),
        ((0, 0), (1, 1)),
        dimension_numbers=("CHWN", "IHWO", "HWCN"),
        preferred_element_type=jnp.float32,
    )
    grad = jnp.flip(grad, (0, 1))
    return grad.reshape(-1, grad.shape[-1])


def silu_slope(preact):
    sigma = jax.nn.sigmoid(preact)
    return sigma * (1.0 + preact * (1.0 - sigma))


def rim(stacked):
    return extended_2(stacked, (("space", 1),), 1)


def send_both(distance, stacked):
    return jax.tree.map(
        lambda part, own: part.astype(own.dtype),
        passed_along(as_sent(stacked), "replica", distance),
        stacked,
    )


def gossip(step, stacked, sender):
    levels = lax.axis_size("replica").bit_length() - 1
    received = lax.switch(
        step[0] % levels, [partial(sender, 1 << power) for power in range(levels)], stacked
    )
    return 0.5 * (stacked + received)


def gathered(weights, which):
    return lax.all_gather(weights[0, which].astype(jnp.bfloat16), "space", axis=0, tiled=True)


def scattered(grad):
    return lax.psum_scatter(
        grad.astype(jnp.bfloat16), "space", scatter_dimension=0, tiled=True
    ).astype(jnp.float32)


def shards(inputs, cotangent, land_mask, weights, momentum, step):
    row_count = inputs.shape[1]
    col_count = inputs.shape[2]
    space_count = lax.axis_size("space")
    scale = 1.0 / math.sqrt(row_count * space_count * col_count)
    masked = cotangent[0] * land_mask.astype(jnp.bfloat16)[:, :, None]
    kernel_first = gathered(weights, 0)
    kernel_second = gathered(weights, 1)
    paired = rim(jnp.stack([inputs[0], masked]))
    input_ext = paired[0]
    masked_ext = paired[1]
    preact = conv_ahead(input_ext, kernel_first)
    hidden = jax.nn.silu(preact).astype(jnp.bfloat16)
    share_second = scattered(kernel_grad_behind(masked_ext, hidden) * scale)
    back_mid = (conv_behind(masked_ext, kernel_second) * silu_slope(preact)).astype(jnp.bfloat16)
    share_first = scattered(kernel_grad(input_ext, back_mid) * scale)
    back_ext = rim(back_mid[None])[0]
    grad_input = (conv_behind(back_ext, kernel_first) + masked.astype(jnp.float32)).astype(
        jnp.bfloat16
    )[None]
    shares = jnp.stack([share_first, share_second])[None]
    moment = 0.9 * momentum + shares
    updated = weights - 0.01 * moment
    mixed = gossip(step, jnp.stack([updated, moment]), send_both)
    new_weights = mixed[0]
    new_momentum = mixed[1]
    return (grad_input, new_weights, new_momentum)


def solution(mesh):
    in_specs = (
        P("replica", "space", None, None),
        P("replica", "space", None, None),
        P("space", None),
        P("replica", None, "space", None),
        P("replica", None, "space", None),
        P(),
    )
    out_specs = (
        P("replica", "space", None, None),
        P("replica", None, "space", None),
        P("replica", None, "space", None),
    )
    return jax.shard_map(shards, mesh=mesh, in_specs=in_specs, out_specs=out_specs, check_vma=False)
```

```python
from functools import partial
import math

import jax
import jax.numpy as jnp
from jax import lax
from jax.sharding import PartitionSpec as P


def extended_2(shard, sides, width):
    for axis, dim in sides:
        size, length = (lax.axis_size(axis), shard.shape[dim])
        up = [(i, (i + 1) % size) for i in range(size - 1)]
        down = [(j, i) for i, j in up]
        last = lax.slice_in_dim(shard, length - width, length, axis=dim)
        initial = lax.slice_in_dim(shard, 0, width, axis=dim)
        before = lax.ppermute(last, axis, up)
        after = lax.ppermute(initial, axis, down)
        shard = jnp.concatenate([before, shard, after], axis=dim)
    return shard


def as_sent(shard):

    def short(part):
        return part.astype(jnp.bfloat16) if part.dtype == jnp.float32 else part

    return jax.tree.map(short, shard)


def passed_along(shard, axis, by):
    length = lax.axis_size(axis)
    return lax.ppermute(shard, axis, [(i, (i + by) % length) for i in range(length)])


def conv_ahead(extended, kernel):
    chan_count = extended.shape[-1]
    taps = kernel.reshape(3, 3, chan_count, kernel.shape[1])
    return lax.conv_general_dilated(
        extended[None],
        taps,
        (1, 1),
        ((0, 0), (1, 1)),
        dimension_numbers=("NHWC", "HWIO", "NHWC"),
        preferred_element_type=jnp.float32,
    )[0]


def conv_behind(extended, kernel):
    chan_count = kernel.shape[0] // 9
    taps = jnp.flip(kernel.reshape(3, 3, chan_count, kernel.shape[1]), (0, 1))
    return lax.conv_general_dilated(
        extended[None],
        taps,
        (1, 1),
        ((0, 0), (1, 1)),
        dimension_numbers=("NHWC", "HWOI", "NHWC"),
        preferred_element_type=jnp.float32,
    )[0]


def kernel_grad(extended, upstream):
    grad = lax.conv_general_dilated(
        extended[None],
        upstream[None],
        (1, 1),
        ((0, 0), (1, 1)),
        dimension_numbers=("CHWN", "IHWO", "HWNC"),
        preferred_element_type=jnp.float32,
    )
    return grad.reshape(-1, grad.shape[-1])


def kernel_grad_behind(extended_upstream, field):
    grad = lax.conv_general_dilated(
        extended_upstream[None],
        field[None],
        (1, 1),
        ((0, 0), (1, 1)),
        dimension_numbers=("CHWN", "IHWO", "HWCN"),
        preferred_element_type=jnp.float32,
    )
    grad = jnp.flip(grad, (0, 1))
    return grad.reshape(-1, grad.shape[-1])


def silu_slope(preact):
    sigma = jax.nn.sigmoid(preact)
    return sigma * (1.0 + preact * (1.0 - sigma))


def rim(stacked):
    return extended_2(stacked, (("space", 1),), 1)


def send_both(distance, stacked):
    return jax.tree.map(
        lambda part, own: part.astype(own.dtype),
        passed_along(as_sent(stacked), "replica", distance),
        stacked,
    )


def gossip(step, stacked, sender):
    levels = lax.axis_size("replica").bit_length() - 1
    received = lax.switch(
        step[0] % levels, [partial(sender, 1 << power) for power in range(levels)], stacked
    )
    return 0.5 * (stacked + received)


def swapped(part, bit):
    count = lax.axis_size("space")
    return lax.ppermute(part, "space", [(i, i ^ (1 << bit)) for i in range(count)])


def space_bits():
    return lax.axis_size("space").bit_length() - 1


def gathered_kernels(weights):
    own = lax.axis_index("space")
    have = weights[0].astype(jnp.bfloat16)[None]
    for bit in reversed(range(space_bits())):
        theirs = swapped(have, bit)
        upper = (own >> bit) & 1
        first = jnp.where(upper == 1, theirs, have)
        second = jnp.where(upper == 1, have, theirs)
        have = jnp.stack([first, second], axis=1).reshape((-1,) + have.shape[1:])
    kernels = jnp.moveaxis(have, 0, 1)
    return kernels.reshape(kernels.shape[0], -1, kernels.shape[-1])


def scattered(grad):
    own = lax.axis_index("space")
    count = lax.axis_size("space")
    left = grad.reshape((count, -1) + grad.shape[1:])
    for bit in range(space_bits()):
        pairs = left.reshape((-1, 2) + left.shape[1:])
        upper = (own >> bit) & 1
        keep = lax.dynamic_index_in_dim(pairs, upper, axis=1, keepdims=False)
        send = lax.dynamic_index_in_dim(pairs, 1 - upper, axis=1, keepdims=False)
        left = keep + swapped(send.astype(jnp.bfloat16), bit).astype(jnp.float32)
    return left[0]


def shards(inputs, cotangent, land_mask, weights, momentum, step):
    row_count = inputs.shape[1]
    col_count = inputs.shape[2]
    space_count = lax.axis_size("space")
    scale = 1.0 / math.sqrt(row_count * space_count * col_count)
    masked = cotangent[0] * land_mask.astype(jnp.bfloat16)[:, :, None]
    kernels = gathered_kernels(weights)
    kernel_first = kernels[0]
    kernel_second = kernels[1]
    paired = rim(jnp.stack([inputs[0], masked]))
    input_ext = paired[0]
    masked_ext = paired[1]
    preact = conv_ahead(input_ext, kernel_first)
    hidden = jax.nn.silu(preact).astype(jnp.bfloat16)
    share_second = scattered(kernel_grad_behind(masked_ext, hidden) * scale)
    back_mid = (conv_behind(masked_ext, kernel_second) * silu_slope(preact)).astype(jnp.bfloat16)
    share_first = scattered(kernel_grad(input_ext, back_mid) * scale)
    back_ext = rim(back_mid[None])[0]
    grad_input = (conv_behind(back_ext, kernel_first) + masked.astype(jnp.float32)).astype(
        jnp.bfloat16
    )[None]
    shares = jnp.stack([share_first, share_second])[None]
    moment = 0.9 * momentum + shares
    updated = weights - 0.01 * moment
    mixed = gossip(step, jnp.stack([updated, moment]), send_both)
    new_weights = mixed[0]
    new_momentum = mixed[1]
    return (grad_input, new_weights, new_momentum)


def solution(mesh):
    in_specs = (
        P("replica", "space", None, None),
        P("replica", "space", None, None),
        P("space", None),
        P("replica", None, "space", None),
        P("replica", None, "space", None),
        P(),
    )
    out_specs = (
        P("replica", "space", None, None),
        P("replica", None, "space", None),
        P("replica", None, "space", None),
    )
    return jax.shard_map(shards, mesh=mesh, in_specs=in_specs, out_specs=out_specs, check_vma=False)
```

```python
from functools import partial
import math

import jax
import jax.numpy as jnp
from jax import lax
from jax.sharding import PartitionSpec as P


def extended_2(shard, sides, width):
    for axis, dim in sides:
        size, length = (lax.axis_size(axis), shard.shape[dim])
        up = [(i, (i + 1) % size) for i in range(size - 1)]
        down = [(j, i) for i, j in up]
        last = lax.slice_in_dim(shard, length - width, length, axis=dim)
        initial = lax.slice_in_dim(shard, 0, width, axis=dim)
        before = lax.ppermute(last, axis, up)
        after = lax.ppermute(initial, axis, down)
        shard = jnp.concatenate([before, shard, after], axis=dim)
    return shard


def as_sent(shard):

    def short(part):
        return part.astype(jnp.bfloat16) if part.dtype == jnp.float32 else part

    return jax.tree.map(short, shard)


def passed_along(shard, axis, by):
    length = lax.axis_size(axis)
    return lax.ppermute(shard, axis, [(i, (i + by) % length) for i in range(length)])


def conv_ahead(extended, kernel):
    chan_count = extended.shape[-1]
    taps = kernel.reshape(3, 3, chan_count, kernel.shape[1])
    return lax.conv_general_dilated(
        extended[None],
        taps,
        (1, 1),
        ((0, 0), (1, 1)),
        dimension_numbers=("NHWC", "HWIO", "NHWC"),
        preferred_element_type=jnp.float32,
    )[0]


def conv_behind(extended, kernel):
    chan_count = kernel.shape[0] // 9
    taps = jnp.flip(kernel.reshape(3, 3, chan_count, kernel.shape[1]), (0, 1))
    return lax.conv_general_dilated(
        extended[None],
        taps,
        (1, 1),
        ((0, 0), (1, 1)),
        dimension_numbers=("NHWC", "HWOI", "NHWC"),
        preferred_element_type=jnp.float32,
    )[0]


def kernel_grad(extended, upstream):
    grad = lax.conv_general_dilated(
        extended[None],
        upstream[None],
        (1, 1),
        ((0, 0), (1, 1)),
        dimension_numbers=("CHWN", "IHWO", "HWNC"),
        preferred_element_type=jnp.float32,
    )
    return grad.reshape(-1, grad.shape[-1])


def kernel_grad_behind(extended_upstream, field):
    grad = lax.conv_general_dilated(
        extended_upstream[None],
        field[None],
        (1, 1),
        ((0, 0), (1, 1)),
        dimension_numbers=("CHWN", "IHWO", "HWCN"),
        preferred_element_type=jnp.float32,
    )
    grad = jnp.flip(grad, (0, 1))
    return grad.reshape(-1, grad.shape[-1])


def silu_slope(preact):
    sigma = jax.nn.sigmoid(preact)
    return sigma * (1.0 + preact * (1.0 - sigma))


def rim(stacked):
    return extended_2(stacked, (("space", 1),), 1)


def send_both(distance, stacked):
    return jax.tree.map(
        lambda part, own: part.astype(own.dtype),
        passed_along(as_sent(stacked), "replica", distance),
        stacked,
    )


def gossip(step, stacked, sender):
    levels = lax.axis_size("replica").bit_length() - 1
    received = lax.switch(
        step[0] % levels, [partial(sender, 1 << power) for power in range(levels)], stacked
    )
    return 0.5 * (stacked + received)


def swapped(part, bit):
    count = lax.axis_size("space")
    return lax.ppermute(part, "space", [(i, i ^ (1 << bit)) for i in range(count)])


def space_bits():
    return lax.axis_size("space").bit_length() - 1


def gathered_kernels(weights):
    own = lax.axis_index("space")
    have = weights[0].astype(jnp.bfloat16)[None]
    for bit in reversed(range(space_bits())):
        theirs = swapped(have, bit)
        upper = (own >> bit) & 1
        first = jnp.where(upper == 1, theirs, have)
        second = jnp.where(upper == 1, have, theirs)
        have = jnp.stack([first, second], axis=1).reshape((-1,) + have.shape[1:])
    kernels = jnp.moveaxis(have, 0, 1)
    return kernels.reshape(kernels.shape[0], -1, kernels.shape[-1])


def scattered(grad):
    count = lax.axis_size("space")
    blocks = grad.reshape((grad.shape[0], count, -1) + grad.shape[2:])
    received = lax.all_to_all(
        jnp.moveaxis(blocks, 1, 0).astype(jnp.bfloat16), "space", 0, 0, tiled=True
    )
    return jnp.sum(received.astype(jnp.float32), axis=0)


def shards(inputs, cotangent, land_mask, weights, momentum, step):
    row_count = inputs.shape[1]
    col_count = inputs.shape[2]
    space_count = lax.axis_size("space")
    scale = 1.0 / math.sqrt(row_count * space_count * col_count)
    masked = cotangent[0] * land_mask.astype(jnp.bfloat16)[:, :, None]
    kernels = gathered_kernels(weights)
    kernel_first = kernels[0]
    kernel_second = kernels[1]
    paired = rim(jnp.stack([inputs[0], masked]))
    input_ext = paired[0]
    masked_ext = paired[1]
    preact = conv_ahead(input_ext, kernel_first)
    hidden = jax.nn.silu(preact).astype(jnp.bfloat16)
    grad_second = kernel_grad_behind(masked_ext, hidden) * scale
    back_mid = (conv_behind(masked_ext, kernel_second) * silu_slope(preact)).astype(jnp.bfloat16)
    grad_first = kernel_grad(input_ext, back_mid) * scale
    back_ext = rim(back_mid[None])[0]
    grad_input = (conv_behind(back_ext, kernel_first) + masked.astype(jnp.float32)).astype(
        jnp.bfloat16
    )[None]
    shares = scattered(jnp.stack([grad_first, grad_second]))[None]
    moment = 0.9 * momentum + shares
    updated = weights - 0.01 * moment
    mixed = gossip(step, jnp.stack([updated, moment]), send_both)
    new_weights = mixed[0]
    new_momentum = mixed[1]
    return (grad_input, new_weights, new_momentum)


def solution(mesh):
    in_specs = (
        P("replica", "space", None, None),
        P("replica", "space", None, None),
        P("space", None),
        P("replica", None, "space", None),
        P("replica", None, "space", None),
        P(),
    )
    out_specs = (
        P("replica", "space", None, None),
        P("replica", None, "space", None),
        P("replica", None, "space", None),
    )
    return jax.shard_map(shards, mesh=mesh, in_specs=in_specs, out_specs=out_specs, check_vma=False)
```

```python
from functools import partial
import math

import jax
import jax.numpy as jnp
from jax import lax
from jax.sharding import PartitionSpec as P


def extended_2(shard, sides, width):
    for axis, dim in sides:
        size, length = (lax.axis_size(axis), shard.shape[dim])
        up = [(i, (i + 1) % size) for i in range(size - 1)]
        down = [(j, i) for i, j in up]
        last = lax.slice_in_dim(shard, length - width, length, axis=dim)
        initial = lax.slice_in_dim(shard, 0, width, axis=dim)
        before = lax.ppermute(last, axis, up)
        after = lax.ppermute(initial, axis, down)
        shard = jnp.concatenate([before, shard, after], axis=dim)
    return shard


def as_sent(shard):

    def short(part):
        return part.astype(jnp.bfloat16) if part.dtype == jnp.float32 else part

    return jax.tree.map(short, shard)


def passed_along(shard, axis, by):
    length = lax.axis_size(axis)
    return lax.ppermute(shard, axis, [(i, (i + by) % length) for i in range(length)])


def conv_ahead(extended, kernel):
    chan_count = extended.shape[-1]
    taps = kernel.reshape(3, 3, chan_count, kernel.shape[1])
    return lax.conv_general_dilated(
        extended[None],
        taps,
        (1, 1),
        ((0, 0), (1, 1)),
        dimension_numbers=("NHWC", "HWIO", "NHWC"),
        preferred_element_type=jnp.float32,
    )[0]


def conv_behind(extended, kernel):
    chan_count = kernel.shape[0] // 9
    taps = jnp.flip(kernel.reshape(3, 3, chan_count, kernel.shape[1]), (0, 1))
    return lax.conv_general_dilated(
        extended[None],
        taps,
        (1, 1),
        ((0, 0), (1, 1)),
        dimension_numbers=("NHWC", "HWOI", "NHWC"),
        preferred_element_type=jnp.float32,
    )[0]


def kernel_grad(extended, upstream):
    grad = lax.conv_general_dilated(
        extended[None],
        upstream[None],
        (1, 1),
        ((0, 0), (1, 1)),
        dimension_numbers=("CHWN", "IHWO", "HWNC"),
        preferred_element_type=jnp.float32,
    )
    return grad.reshape(-1, grad.shape[-1])


def kernel_grad_behind(extended_upstream, field):
    grad = lax.conv_general_dilated(
        extended_upstream[None],
        field[None],
        (1, 1),
        ((0, 0), (1, 1)),
        dimension_numbers=("CHWN", "IHWO", "HWCN"),
        preferred_element_type=jnp.float32,
    )
    grad = jnp.flip(grad, (0, 1))
    return grad.reshape(-1, grad.shape[-1])


def silu_slope(preact):
    sigma = jax.nn.sigmoid(preact)
    return sigma * (1.0 + preact * (1.0 - sigma))


def rim(stacked):
    return extended_2(stacked, (("space", 1),), 1)


def send_both(distance, stacked):
    return jax.tree.map(
        lambda part, own: part.astype(own.dtype),
        passed_along(as_sent(stacked), "replica", distance),
        stacked,
    )


def gossip(step, stacked, sender):
    levels = lax.axis_size("replica").bit_length() - 1
    received = lax.switch(
        step[0] % levels, [partial(sender, 1 << power) for power in range(levels)], stacked
    )
    return 0.5 * (stacked + received)


def swapped(part, bit):
    count = lax.axis_size("space")
    return lax.ppermute(part, "space", [(i, i ^ (1 << bit)) for i in range(count)])


def space_bits():
    return lax.axis_size("space").bit_length() - 1


def gathered_kernels(weights):
    own = lax.axis_index("space")
    have = weights[0].astype(jnp.bfloat16)[None]
    for bit in reversed(range(space_bits())):
        theirs = swapped(have, bit)
        upper = (own >> bit) & 1
        first = jnp.where(upper == 1, theirs, have)
        second = jnp.where(upper == 1, have, theirs)
        have = jnp.stack([first, second], axis=1).reshape((-1,) + have.shape[1:])
    kernels = jnp.moveaxis(have, 0, 1)
    return kernels.reshape(kernels.shape[0], -1, kernels.shape[-1])


def scattered(grad):
    count = lax.axis_size("space")
    blocks = grad.reshape((grad.shape[0], count, -1) + grad.shape[2:])
    received = lax.all_to_all(
        jnp.moveaxis(blocks, 1, 0).astype(jnp.bfloat16), "space", 0, 0, tiled=True
    )
    return jnp.sum(received.astype(jnp.float32), axis=0)


def shards(inputs, cotangent, land_mask, weights, momentum, step):
    row_count = inputs.shape[1]
    col_count = inputs.shape[2]
    space_count = lax.axis_size("space")
    scale = 1.0 / math.sqrt(row_count * space_count * col_count)
    masked = cotangent[0] * land_mask.astype(jnp.bfloat16)[:, :, None]
    kernels = gathered_kernels(weights)
    kernel_first = kernels[0]
    kernel_second = kernels[1]
    paired = rim(jnp.stack([inputs[0], masked]))
    input_ext = paired[0]
    masked_ext = paired[1]
    preact = conv_ahead(input_ext, kernel_first)
    hidden = jax.nn.silu(preact).astype(jnp.bfloat16)
    grad_second = kernel_grad_behind(masked_ext, hidden) * scale
    back_mid = (conv_behind(masked_ext, kernel_second) * silu_slope(preact)).astype(jnp.bfloat16)
    grad_first = kernel_grad(input_ext, back_mid) * scale
    back_ext, grad_first, grad_second = lax.optimization_barrier(
        (rim(back_mid[None])[0], grad_first, grad_second)
    )
    grad_input = (conv_behind(back_ext, kernel_first) + masked.astype(jnp.float32)).astype(
        jnp.bfloat16
    )[None]
    shares = scattered(jnp.stack([grad_first, grad_second]))[None]
    moment = 0.9 * momentum + shares
    updated = weights - 0.01 * moment
    mixed = gossip(step, jnp.stack([updated, moment]), send_both)
    new_weights = mixed[0]
    new_momentum = mixed[1]
    return (grad_input, new_weights, new_momentum)


def solution(mesh):
    in_specs = (
        P("replica", "space", None, None),
        P("replica", "space", None, None),
        P("space", None),
        P("replica", None, "space", None),
        P("replica", None, "space", None),
        P(),
    )
    out_specs = (
        P("replica", "space", None, None),
        P("replica", None, "space", None),
        P("replica", None, "space", None),
    )
    return jax.shard_map(shards, mesh=mesh, in_specs=in_specs, out_specs=out_specs, check_vma=False)
```

```python
from functools import partial
import math

import jax
import jax.numpy as jnp
from jax import lax
from jax.sharding import PartitionSpec as P


def extended_2(shard, sides, width):
    for axis, dim in sides:
        size, length = (lax.axis_size(axis), shard.shape[dim])
        up = [(i, (i + 1) % size) for i in range(size - 1)]
        down = [(j, i) for i, j in up]
        last = lax.slice_in_dim(shard, length - width, length, axis=dim)
        initial = lax.slice_in_dim(shard, 0, width, axis=dim)
        before = lax.ppermute(last, axis, up)
        after = lax.ppermute(initial, axis, down)
        shard = jnp.concatenate([before, shard, after], axis=dim)
    return shard


def as_sent(shard):

    def short(part):
        return part.astype(jnp.bfloat16) if part.dtype == jnp.float32 else part

    return jax.tree.map(short, shard)


def passed_along(shard, axis, by):
    length = lax.axis_size(axis)
    return lax.ppermute(shard, axis, [(i, (i + by) % length) for i in range(length)])


def conv_ahead(extended, kernel):
    chan_count = extended.shape[-1]
    taps = kernel.reshape(3, 3, chan_count, kernel.shape[1])
    return lax.conv_general_dilated(
        extended[None],
        taps,
        (1, 1),
        ((0, 0), (1, 1)),
        dimension_numbers=("NHWC", "HWIO", "NHWC"),
        preferred_element_type=jnp.float32,
    )[0]


def conv_behind(extended, kernel):
    chan_count = kernel.shape[0] // 9
    taps = jnp.flip(kernel.reshape(3, 3, chan_count, kernel.shape[1]), (0, 1))
    return lax.conv_general_dilated(
        extended[None],
        taps,
        (1, 1),
        ((0, 0), (1, 1)),
        dimension_numbers=("NHWC", "HWOI", "NHWC"),
        preferred_element_type=jnp.float32,
    )[0]


def kernel_grad(extended, upstream):
    grad = lax.conv_general_dilated(
        extended[None],
        upstream[None],
        (1, 1),
        ((0, 0), (1, 1)),
        dimension_numbers=("CHWN", "IHWO", "HWNC"),
        preferred_element_type=jnp.float32,
    )
    return grad.reshape(-1, grad.shape[-1])


def kernel_grad_behind(extended_upstream, field):
    grad = lax.conv_general_dilated(
        extended_upstream[None],
        field[None],
        (1, 1),
        ((0, 0), (1, 1)),
        dimension_numbers=("CHWN", "IHWO", "HWCN"),
        preferred_element_type=jnp.float32,
    )
    grad = jnp.flip(grad, (0, 1))
    return grad.reshape(-1, grad.shape[-1])


def silu_slope(preact):
    sigma = jax.nn.sigmoid(preact)
    return sigma * (1.0 + preact * (1.0 - sigma))


def rim(stacked):
    return extended_2(stacked, (("space", 1),), 1)


def send_both(distance, stacked):
    return jax.tree.map(
        lambda part, own: part.astype(own.dtype),
        passed_along(as_sent(stacked), "replica", distance),
        stacked,
    )


def gossip(step, stacked, sender):
    levels = lax.axis_size("replica").bit_length() - 1
    received = lax.switch(
        step[0] % levels, [partial(sender, 1 << power) for power in range(levels)], stacked
    )
    return 0.5 * (stacked + received)


def swapped(part, bit):
    count = lax.axis_size("space")
    return lax.ppermute(part, "space", [(i, i ^ (1 << bit)) for i in range(count)])


def space_bits():
    return lax.axis_size("space").bit_length() - 1


def gathered_kernels(weights):
    count = lax.axis_size("space")
    own = weights[0].astype(jnp.bfloat16)
    copies = jnp.broadcast_to(own[None], (count,) + own.shape)
    have = lax.all_to_all(copies, "space", 0, 0, tiled=True)
    kernels = jnp.moveaxis(have, 0, 1)
    return kernels.reshape(kernels.shape[0], -1, kernels.shape[-1])


def scattered(grad):
    count = lax.axis_size("space")
    blocks = grad.reshape((grad.shape[0], count, -1) + grad.shape[2:])
    received = lax.all_to_all(
        jnp.moveaxis(blocks, 1, 0).astype(jnp.bfloat16), "space", 0, 0, tiled=True
    )
    return jnp.sum(received.astype(jnp.float32), axis=0)


def shards(inputs, cotangent, land_mask, weights, momentum, step):
    row_count = inputs.shape[1]
    col_count = inputs.shape[2]
    space_count = lax.axis_size("space")
    scale = 1.0 / math.sqrt(row_count * space_count * col_count)
    masked = cotangent[0] * land_mask.astype(jnp.bfloat16)[:, :, None]
    kernels = gathered_kernels(weights)
    kernel_first = kernels[0]
    kernel_second = kernels[1]
    paired = rim(jnp.stack([inputs[0], masked]))
    input_ext = paired[0]
    masked_ext = paired[1]
    preact = conv_ahead(input_ext, kernel_first)
    hidden = jax.nn.silu(preact).astype(jnp.bfloat16)
    grad_second = kernel_grad_behind(masked_ext, hidden) * scale
    back_mid = (conv_behind(masked_ext, kernel_second) * silu_slope(preact)).astype(jnp.bfloat16)
    grad_first = kernel_grad(input_ext, back_mid) * scale
    back_ext, grad_first, grad_second = lax.optimization_barrier(
        (rim(back_mid[None])[0], grad_first, grad_second)
    )
    grad_input = (conv_behind(back_ext, kernel_first) + masked.astype(jnp.float32)).astype(
        jnp.bfloat16
    )[None]
    shares = scattered(jnp.stack([grad_first, grad_second]))[None]
    moment = 0.9 * momentum + shares
    updated = weights - 0.01 * moment
    mixed = gossip(step, jnp.stack([updated, moment]), send_both)
    new_weights = mixed[0]
    new_momentum = mixed[1]
    return (grad_input, new_weights, new_momentum)


def solution(mesh):
    in_specs = (
        P("replica", "space", None, None),
        P("replica", "space", None, None),
        P("space", None),
        P("replica", None, "space", None),
        P("replica", None, "space", None),
        P(),
    )
    out_specs = (
        P("replica", "space", None, None),
        P("replica", None, "space", None),
        P("replica", None, "space", None),
    )
    return jax.shard_map(shards, mesh=mesh, in_specs=in_specs, out_specs=out_specs, check_vma=False)
```

```python
from functools import partial
import math

import jax
import jax.numpy as jnp
from jax import lax
from jax.sharding import PartitionSpec as P


def extended_2(shard, sides, width):
    for axis, dim in sides:
        size, length = (lax.axis_size(axis), shard.shape[dim])
        up = [(i, (i + 1) % size) for i in range(size - 1)]
        down = [(j, i) for i, j in up]
        last = lax.slice_in_dim(shard, length - width, length, axis=dim)
        initial = lax.slice_in_dim(shard, 0, width, axis=dim)
        before = lax.ppermute(last, axis, up)
        after = lax.ppermute(initial, axis, down)
        shard = jnp.concatenate([before, shard, after], axis=dim)
    return shard


def as_sent(shard):

    def short(part):
        return part.astype(jnp.bfloat16) if part.dtype == jnp.float32 else part

    return jax.tree.map(short, shard)


def passed_along(shard, axis, by):
    length = lax.axis_size(axis)
    return lax.ppermute(shard, axis, [(i, (i + by) % length) for i in range(length)])


def conv_ahead(extended, kernel):
    chan_count = extended.shape[-1]
    taps = kernel.reshape(3, 3, chan_count, kernel.shape[1])
    return lax.conv_general_dilated(
        extended[None],
        taps,
        (1, 1),
        ((0, 0), (1, 1)),
        dimension_numbers=("NHWC", "HWIO", "NHWC"),
        preferred_element_type=jnp.float32,
    )[0]


def conv_behind(extended, kernel):
    chan_count = kernel.shape[0] // 9
    taps = jnp.flip(kernel.reshape(3, 3, chan_count, kernel.shape[1]), (0, 1))
    return lax.conv_general_dilated(
        extended[None],
        taps,
        (1, 1),
        ((0, 0), (1, 1)),
        dimension_numbers=("NHWC", "HWOI", "NHWC"),
        preferred_element_type=jnp.float32,
    )[0]


def kernel_grad(extended, upstream):
    grad = lax.conv_general_dilated(
        extended[None],
        upstream[None],
        (1, 1),
        ((0, 0), (1, 1)),
        dimension_numbers=("CHWN", "IHWO", "HWNC"),
        preferred_element_type=jnp.float32,
    )
    return grad.reshape(-1, grad.shape[-1])


def kernel_grad_behind(extended_upstream, field):
    grad = lax.conv_general_dilated(
        extended_upstream[None],
        field[None],
        (1, 1),
        ((0, 0), (1, 1)),
        dimension_numbers=("CHWN", "IHWO", "HWCN"),
        preferred_element_type=jnp.float32,
    )
    grad = jnp.flip(grad, (0, 1))
    return grad.reshape(-1, grad.shape[-1])


def silu_slope(preact):
    sigma = jax.nn.sigmoid(preact)
    return sigma * (1.0 + preact * (1.0 - sigma))


def rim(stacked):
    return extended_2(stacked, (("space", 1),), 1)


def send_both(distance, stacked):
    return jax.tree.map(
        lambda part, own: part.astype(own.dtype),
        passed_along(as_sent(stacked), "replica", distance),
        stacked,
    )


def gossip(step, stacked, sender):
    levels = lax.axis_size("replica").bit_length() - 1
    received = lax.switch(
        step[0] % levels, [partial(sender, 1 << power) for power in range(levels)], stacked
    )
    return 0.5 * (stacked + received)


def swapped(part, bit):
    count = lax.axis_size("space")
    return lax.ppermute(part, "space", [(i, i ^ (1 << bit)) for i in range(count)])


def space_bits():
    return lax.axis_size("space").bit_length() - 1


def gathered_kernels(weights):
    count = lax.axis_size("space")
    own = weights[0].astype(jnp.bfloat16)
    copies = jnp.broadcast_to(own[None], (count,) + own.shape)
    have = lax.all_to_all(copies, "space", 0, 0, tiled=True)
    kernels = jnp.moveaxis(have, 0, 1)
    return kernels.reshape(kernels.shape[0], -1, kernels.shape[-1])


def scattered(grad):
    count = lax.axis_size("space")
    blocks = grad.reshape((grad.shape[0], count, -1) + grad.shape[2:])
    received = lax.all_to_all(
        jnp.moveaxis(blocks, 1, 0).astype(jnp.bfloat16), "space", 0, 0, tiled=True
    )
    return jnp.sum(received.astype(jnp.float32), axis=0)


def shards(inputs, cotangent, land_mask, weights, momentum, step):
    row_count = inputs.shape[1]
    col_count = inputs.shape[2]
    space_count = lax.axis_size("space")
    scale = 1.0 / math.sqrt(row_count * space_count * col_count)
    masked = cotangent[0] * land_mask.astype(jnp.bfloat16)[:, :, None]
    kernels = gathered_kernels(weights)
    kernel_first = kernels[0]
    kernel_second = kernels[1]
    paired = rim(jnp.stack([inputs[0], masked]))
    input_ext = paired[0]
    masked_ext = paired[1]
    preact = conv_ahead(input_ext, kernel_first)
    hidden = jax.nn.silu(preact).astype(jnp.bfloat16)
    share_second = scattered(kernel_grad_behind(masked_ext, hidden)[None] * scale)
    back_mid = (conv_behind(masked_ext, kernel_second) * silu_slope(preact)).astype(jnp.bfloat16)
    grad_first = kernel_grad(input_ext, back_mid) * scale
    back_ext, grad_first = lax.optimization_barrier((rim(back_mid[None])[0], grad_first))
    grad_input = (conv_behind(back_ext, kernel_first) + masked.astype(jnp.float32)).astype(
        jnp.bfloat16
    )[None]
    shares = jnp.stack([scattered(grad_first[None])[0], share_second[0]])[None]
    moment = 0.9 * momentum + shares
    updated = weights - 0.01 * moment
    mixed = gossip(step, jnp.stack([updated, moment]), send_both)
    new_weights = mixed[0]
    new_momentum = mixed[1]
    return (grad_input, new_weights, new_momentum)


def solution(mesh):
    in_specs = (
        P("replica", "space", None, None),
        P("replica", "space", None, None),
        P("space", None),
        P("replica", None, "space", None),
        P("replica", None, "space", None),
        P(),
    )
    out_specs = (
        P("replica", "space", None, None),
        P("replica", None, "space", None),
        P("replica", None, "space", None),
    )
    return jax.shard_map(shards, mesh=mesh, in_specs=in_specs, out_specs=out_specs, check_vma=False)
```

```python
from functools import partial
import math

import jax
import jax.numpy as jnp
from jax import lax
from jax.sharding import PartitionSpec as P


def extended_2(shard, sides, width):
    for axis, dim in sides:
        size, length = (lax.axis_size(axis), shard.shape[dim])
        up = [(i, (i + 1) % size) for i in range(size - 1)]
        down = [(j, i) for i, j in up]
        last = lax.slice_in_dim(shard, length - width, length, axis=dim)
        initial = lax.slice_in_dim(shard, 0, width, axis=dim)
        before = lax.ppermute(last, axis, up)
        after = lax.ppermute(initial, axis, down)
        shard = jnp.concatenate([before, shard, after], axis=dim)
    return shard


def as_sent(shard):

    def short(part):
        return part.astype(jnp.bfloat16) if part.dtype == jnp.float32 else part

    return jax.tree.map(short, shard)


def passed_along(shard, axis, by):
    length = lax.axis_size(axis)
    return lax.ppermute(shard, axis, [(i, (i + by) % length) for i in range(length)])


def conv_ahead(extended, kernel):
    chan_count = extended.shape[-1]
    taps = kernel.reshape(3, 3, chan_count, kernel.shape[1])
    return lax.conv_general_dilated(
        extended[None],
        taps,
        (1, 1),
        ((0, 0), (1, 1)),
        dimension_numbers=("NHWC", "HWIO", "NHWC"),
        preferred_element_type=jnp.float32,
    )[0]


def conv_behind(extended, kernel):
    chan_count = kernel.shape[0] // 9
    taps = jnp.flip(kernel.reshape(3, 3, chan_count, kernel.shape[1]), (0, 1))
    return lax.conv_general_dilated(
        extended[None],
        taps,
        (1, 1),
        ((0, 0), (1, 1)),
        dimension_numbers=("NHWC", "HWOI", "NHWC"),
        preferred_element_type=jnp.float32,
    )[0]


def kernel_grad(extended, upstream):
    grad = lax.conv_general_dilated(
        extended[None],
        upstream[None],
        (1, 1),
        ((0, 0), (1, 1)),
        dimension_numbers=("CHWN", "IHWO", "HWNC"),
        preferred_element_type=jnp.float32,
    )
    return grad.reshape(-1, grad.shape[-1])


def kernel_grad_behind(extended_upstream, field):
    grad = lax.conv_general_dilated(
        extended_upstream[None],
        field[None],
        (1, 1),
        ((0, 0), (1, 1)),
        dimension_numbers=("CHWN", "IHWO", "HWCN"),
        preferred_element_type=jnp.float32,
    )
    grad = jnp.flip(grad, (0, 1))
    return grad.reshape(-1, grad.shape[-1])


def both_ahead(extended, kernel_first, kernel_second):
    chan_count = kernel_first.shape[1]
    first = kernel_first.reshape(3, 3, -1, chan_count)
    second = jnp.flip(kernel_second.reshape(3, 3, -1, chan_count), (0, 1)).transpose(0, 1, 3, 2)
    summed = lax.conv_general_dilated(
        extended[None],
        jnp.concatenate([first, second], axis=-1),
        (1, 1),
        ((0, 0), (1, 1)),
        dimension_numbers=("NHWC", "HWIO", "NHWC"),
        feature_group_count=2,
        preferred_element_type=jnp.float32,
    )[0]
    return summed[..., :chan_count], summed[..., chan_count:]


def both_grads(extended, upstream):
    chan_count = extended.shape[-1] // 2
    grad = lax.conv_general_dilated(
        extended[None],
        upstream[None],
        (1, 1),
        ((0, 0), (1, 1)),
        dimension_numbers=("CHWN", "IHWO", "HWNC"),
        batch_group_count=2,
        preferred_element_type=jnp.float32,
    )
    first = grad[..., :chan_count]
    second = jnp.flip(grad[..., chan_count:], (0, 1)).transpose(0, 1, 3, 2)
    return jnp.stack([first.reshape(-1, chan_count), second.reshape(-1, chan_count)])


def silu_slope(preact):
    sigma = jax.nn.sigmoid(preact)
    return sigma * (1.0 + preact * (1.0 - sigma))


def rim(stacked):
    return extended_2(stacked, (("space", 1),), 1)


def send_both(distance, stacked):
    return jax.tree.map(
        lambda part, own: part.astype(own.dtype),
        passed_along(as_sent(stacked), "replica", distance),
        stacked,
    )


def gossip(step, stacked, sender):
    levels = lax.axis_size("replica").bit_length() - 1
    received = lax.switch(
        step[0] % levels, [partial(sender, 1 << power) for power in range(levels)], stacked
    )
    return 0.5 * (stacked + received)


def swapped(part, bit):
    count = lax.axis_size("space")
    return lax.ppermute(part, "space", [(i, i ^ (1 << bit)) for i in range(count)])


def space_bits():
    return lax.axis_size("space").bit_length() - 1


def gathered_kernels(weights):
    count = lax.axis_size("space")
    own = weights[0].astype(jnp.bfloat16)
    copies = jnp.broadcast_to(own[None], (count,) + own.shape)
    have = lax.all_to_all(copies, "space", 0, 0, tiled=True)
    kernels = jnp.moveaxis(have, 0, 1)
    return kernels.reshape(kernels.shape[0], -1, kernels.shape[-1])


def scattered(grad):
    count = lax.axis_size("space")
    blocks = grad.reshape((grad.shape[0], count, -1) + grad.shape[2:])
    received = lax.all_to_all(
        jnp.moveaxis(blocks, 1, 0).astype(jnp.bfloat16), "space", 0, 0, tiled=True
    )
    return jnp.sum(received.astype(jnp.float32), axis=0)


def shards(inputs, cotangent, land_mask, weights, momentum, step):
    row_count = inputs.shape[1]
    col_count = inputs.shape[2]
    space_count = lax.axis_size("space")
    scale = 1.0 / math.sqrt(row_count * space_count * col_count)
    masked = cotangent[0] * land_mask.astype(jnp.bfloat16)[:, :, None]
    kernels = gathered_kernels(weights)
    kernel_first = kernels[0]
    kernel_second = kernels[1]
    paired = rim(jnp.concatenate([inputs[0], masked], axis=-1)[None])[0]
    preact, back_hidden = both_ahead(paired, kernel_first, kernel_second)
    hidden = jax.nn.silu(preact).astype(jnp.bfloat16)
    back_mid = (back_hidden * silu_slope(preact)).astype(jnp.bfloat16)
    grads = both_grads(paired, jnp.concatenate([back_mid, hidden], axis=-1)) * scale
    back_ext, grads = lax.optimization_barrier((rim(back_mid[None])[0], grads))
    grad_input = (conv_behind(back_ext, kernel_first) + masked.astype(jnp.float32)).astype(
        jnp.bfloat16
    )[None]
    shares = scattered(grads)[None]
    moment = 0.9 * momentum + shares
    updated = weights - 0.01 * moment
    mixed = gossip(step, jnp.stack([updated, moment]), send_both)
    new_weights = mixed[0]
    new_momentum = mixed[1]
    return (grad_input, new_weights, new_momentum)


def solution(mesh):
    in_specs = (
        P("replica", "space", None, None),
        P("replica", "space", None, None),
        P("space", None),
        P("replica", None, "space", None),
        P("replica", None, "space", None),
        P(),
    )
    out_specs = (
        P("replica", "space", None, None),
        P("replica", None, "space", None),
        P("replica", None, "space", None),
    )
    return jax.shard_map(shards, mesh=mesh, in_specs=in_specs, out_specs=out_specs, check_vma=False)
```

```python
from functools import partial
import math

import jax
import jax.numpy as jnp
from jax import lax
from jax.sharding import PartitionSpec as P


def extended_2(shard, sides, width):
    for axis, dim in sides:
        size, length = (lax.axis_size(axis), shard.shape[dim])
        up = [(i, (i + 1) % size) for i in range(size - 1)]
        down = [(j, i) for i, j in up]
        last = lax.slice_in_dim(shard, length - width, length, axis=dim)
        initial = lax.slice_in_dim(shard, 0, width, axis=dim)
        before = lax.ppermute(last, axis, up)
        after = lax.ppermute(initial, axis, down)
        shard = jnp.concatenate([before, shard, after], axis=dim)
    return shard


def as_sent(shard):

    def short(part):
        return part.astype(jnp.bfloat16) if part.dtype == jnp.float32 else part

    return jax.tree.map(short, shard)


def passed_along(shard, axis, by):
    length = lax.axis_size(axis)
    return lax.ppermute(shard, axis, [(i, (i + by) % length) for i in range(length)])


def conv_ahead(extended, kernel):
    chan_count = extended.shape[-1]
    taps = kernel.reshape(3, 3, chan_count, kernel.shape[1])
    return lax.conv_general_dilated(
        extended[None],
        taps,
        (1, 1),
        ((0, 0), (1, 1)),
        dimension_numbers=("NHWC", "HWIO", "NHWC"),
        preferred_element_type=jnp.float32,
    )[0]


def conv_behind(extended, kernel):
    chan_count = kernel.shape[0] // 9
    taps = jnp.flip(kernel.reshape(3, 3, chan_count, kernel.shape[1]), (0, 1))
    return lax.conv_general_dilated(
        extended[None],
        taps,
        (1, 1),
        ((0, 0), (1, 1)),
        dimension_numbers=("NHWC", "HWOI", "NHWC"),
        preferred_element_type=jnp.float32,
    )[0]


def kernel_grad(extended, upstream):
    grad = lax.conv_general_dilated(
        extended[None],
        upstream[None],
        (1, 1),
        ((0, 0), (1, 1)),
        dimension_numbers=("CHWN", "IHWO", "HWNC"),
        preferred_element_type=jnp.float32,
    )
    return grad.reshape(-1, grad.shape[-1])


def kernel_grad_behind(extended_upstream, field):
    grad = lax.conv_general_dilated(
        extended_upstream[None],
        field[None],
        (1, 1),
        ((0, 0), (1, 1)),
        dimension_numbers=("CHWN", "IHWO", "HWCN"),
        preferred_element_type=jnp.float32,
    )
    grad = jnp.flip(grad, (0, 1))
    return grad.reshape(-1, grad.shape[-1])


def silu_slope(preact):
    sigma = jax.nn.sigmoid(preact)
    return sigma * (1.0 + preact * (1.0 - sigma))


def rim(stacked):
    return extended_2(stacked, (("space", 1),), 1)


def send_both(distance, stacked):
    return jax.tree.map(
        lambda part, own: part.astype(own.dtype),
        passed_along(as_sent(stacked), "replica", distance),
        stacked,
    )


def gossip(step, stacked, sender):
    levels = lax.axis_size("replica").bit_length() - 1
    received = lax.switch(
        step[0] % levels, [partial(sender, 1 << power) for power in range(levels)], stacked
    )
    return 0.5 * (stacked + received)


def swapped(part, bit):
    count = lax.axis_size("space")
    return lax.ppermute(part, "space", [(i, i ^ (1 << bit)) for i in range(count)])


def space_bits():
    return lax.axis_size("space").bit_length() - 1


def gathered_kernels(weights):
    return lax.all_gather(weights[0].astype(jnp.bfloat16), "space", axis=1, tiled=True)


def scattered(grad):
    count = lax.axis_size("space")
    blocks = grad.reshape((grad.shape[0], count, -1) + grad.shape[2:])
    received = lax.all_to_all(
        jnp.moveaxis(blocks, 1, 0).astype(jnp.bfloat16), "space", 0, 0, tiled=True
    )
    return jnp.sum(received.astype(jnp.float32), axis=0)


def shards(inputs, cotangent, land_mask, weights, momentum, step):
    row_count = inputs.shape[1]
    col_count = inputs.shape[2]
    space_count = lax.axis_size("space")
    scale = 1.0 / math.sqrt(row_count * space_count * col_count)
    masked = cotangent[0] * land_mask.astype(jnp.bfloat16)[:, :, None]
    kernels = gathered_kernels(weights)
    kernel_first = kernels[0]
    kernel_second = kernels[1]
    paired = rim(jnp.stack([inputs[0], masked]))
    input_ext = paired[0]
    masked_ext = paired[1]
    preact = conv_ahead(input_ext, kernel_first)
    hidden = jax.nn.silu(preact).astype(jnp.bfloat16)
    grad_second = kernel_grad_behind(masked_ext, hidden) * scale
    back_mid = (conv_behind(masked_ext, kernel_second) * silu_slope(preact)).astype(jnp.bfloat16)
    grad_first = kernel_grad(input_ext, back_mid) * scale
    back_ext, grad_first, grad_second = lax.optimization_barrier(
        (rim(back_mid[None])[0], grad_first, grad_second)
    )
    grad_input = (conv_behind(back_ext, kernel_first) + masked.astype(jnp.float32)).astype(
        jnp.bfloat16
    )[None]
    shares = scattered(jnp.stack([grad_first, grad_second]))[None]
    moment = 0.9 * momentum + shares
    updated = weights - 0.01 * moment
    mixed = gossip(step, jnp.stack([updated, moment]), send_both)
    new_weights = mixed[0]
    new_momentum = mixed[1]
    return (grad_input, new_weights, new_momentum)


def solution(mesh):
    in_specs = (
        P("replica", "space", None, None),
        P("replica", "space", None, None),
        P("space", None),
        P("replica", None, "space", None),
        P("replica", None, "space", None),
        P(),
    )
    out_specs = (
        P("replica", "space", None, None),
        P("replica", None, "space", None),
        P("replica", None, "space", None),
    )
    return jax.shard_map(shards, mesh=mesh, in_specs=in_specs, out_specs=out_specs, check_vma=False)
```

```python
from functools import partial
import math

import jax
import jax.numpy as jnp
from jax import lax
from jax.sharding import PartitionSpec as P


def extended_2(shard, sides, width):
    for axis, dim in sides:
        size, length = (lax.axis_size(axis), shard.shape[dim])
        up = [(i, (i + 1) % size) for i in range(size - 1)]
        down = [(j, i) for i, j in up]
        last = lax.slice_in_dim(shard, length - width, length, axis=dim)
        initial = lax.slice_in_dim(shard, 0, width, axis=dim)
        before = lax.ppermute(last, axis, up)
        after = lax.ppermute(initial, axis, down)
        shard = jnp.concatenate([before, shard, after], axis=dim)
    return shard


def as_sent(shard):

    def short(part):
        return part.astype(jnp.bfloat16) if part.dtype == jnp.float32 else part

    return jax.tree.map(short, shard)


def passed_along(shard, axis, by):
    length = lax.axis_size(axis)
    return lax.ppermute(shard, axis, [(i, (i + by) % length) for i in range(length)])


def conv_ahead(extended, kernel):
    chan_count = extended.shape[-1]
    taps = kernel.reshape(3, 3, chan_count, kernel.shape[1])
    return lax.conv_general_dilated(
        extended[None],
        taps,
        (1, 1),
        ((0, 0), (1, 1)),
        dimension_numbers=("NHWC", "HWIO", "NHWC"),
        preferred_element_type=jnp.float32,
    )[0]


def conv_behind(extended, kernel):
    chan_count = kernel.shape[0] // 9
    taps = jnp.flip(kernel.reshape(3, 3, chan_count, kernel.shape[1]), (0, 1))
    return lax.conv_general_dilated(
        extended[None],
        taps,
        (1, 1),
        ((0, 0), (1, 1)),
        dimension_numbers=("NHWC", "HWOI", "NHWC"),
        preferred_element_type=jnp.float32,
    )[0]


def kernel_grad(extended, upstream):
    grad = lax.conv_general_dilated(
        extended[None],
        upstream[None],
        (1, 1),
        ((0, 0), (1, 1)),
        dimension_numbers=("CHWN", "IHWO", "HWNC"),
        preferred_element_type=jnp.float32,
    )
    return grad.reshape(-1, grad.shape[-1])


def kernel_grad_behind(extended_upstream, field):
    grad = lax.conv_general_dilated(
        extended_upstream[None],
        field[None],
        (1, 1),
        ((0, 0), (1, 1)),
        dimension_numbers=("CHWN", "IHWO", "HWCN"),
        preferred_element_type=jnp.float32,
    )
    grad = jnp.flip(grad, (0, 1))
    return grad.reshape(-1, grad.shape[-1])


def silu_slope(preact):
    sigma = jax.nn.sigmoid(preact)
    return sigma * (1.0 + preact * (1.0 - sigma))


def rim(stacked):
    return extended_2(stacked, (("space", 1),), 1)


def send_both(distance, stacked):
    return jax.tree.map(
        lambda part, own: part.astype(own.dtype),
        passed_along(as_sent(stacked), "replica", distance),
        stacked,
    )


def gossip(step, stacked, sender):
    levels = lax.axis_size("replica").bit_length() - 1
    received = lax.switch(
        step[0] % levels, [partial(sender, 1 << power) for power in range(levels)], stacked
    )
    return 0.5 * (stacked + received)


def swapped(part, bit):
    count = lax.axis_size("space")
    return lax.ppermute(part, "space", [(i, i ^ (1 << bit)) for i in range(count)])


def space_bits():
    return lax.axis_size("space").bit_length() - 1


def gathered_kernels(weights):
    count = lax.axis_size("space")
    own = weights[0].astype(jnp.bfloat16)
    copies = jnp.broadcast_to(own[None], (count,) + own.shape)
    have = lax.all_to_all(copies, "space", 0, 0, tiled=True)
    kernels = jnp.moveaxis(have, 0, 1)
    return kernels.reshape(kernels.shape[0], -1, kernels.shape[-1])


def scattered(grad):
    count = lax.axis_size("space")
    blocks = grad.reshape((grad.shape[0], count, -1) + grad.shape[2:])
    received = lax.all_to_all(
        jnp.moveaxis(blocks, 1, 0).astype(jnp.bfloat16), "space", 0, 0, tiled=True
    )
    return jnp.sum(received.astype(jnp.float32), axis=0)


def shards(inputs, cotangent, land_mask, weights, momentum, step):
    row_count = inputs.shape[1]
    col_count = inputs.shape[2]
    space_count = lax.axis_size("space")
    scale = 1.0 / math.sqrt(row_count * space_count * col_count)
    masked = cotangent[0] * land_mask.astype(jnp.bfloat16)[:, :, None]
    kernels = gathered_kernels(weights)
    kernel_first = kernels[0]
    kernel_second = kernels[1]
    paired = extended_2(jnp.stack([inputs[0], masked]), (("space", 1),), 2)
    input_ext = paired[0, 1:-1]
    masked_ext = paired[1, 1:-1]
    preact_wide = conv_ahead(paired[0], kernel_first)
    hidden = jax.nn.silu(preact_wide[1:-1]).astype(jnp.bfloat16)
    grad_second = kernel_grad_behind(masked_ext, hidden) * scale
    back_wide = conv_behind(paired[1], kernel_second) * silu_slope(preact_wide)
    own = lax.axis_index("space")
    rows = jnp.arange(back_wide.shape[0])
    inside = ((rows > 0) | (own > 0)) & ((rows < back_wide.shape[0] - 1) | (own < space_count - 1))
    back_ext = jnp.where(inside[:, None, None], back_wide, 0.0).astype(jnp.bfloat16)
    back_mid = back_ext[1:-1]
    grad_first = kernel_grad(input_ext, back_mid) * scale
    grad_input = (conv_behind(back_ext, kernel_first) + masked.astype(jnp.float32)).astype(
        jnp.bfloat16
    )[None]
    shares = scattered(jnp.stack([grad_first, grad_second]))[None]
    moment = 0.9 * momentum + shares
    updated = weights - 0.01 * moment
    mixed = gossip(step, jnp.stack([updated, moment]), send_both)
    new_weights = mixed[0]
    new_momentum = mixed[1]
    return (grad_input, new_weights, new_momentum)


def solution(mesh):
    in_specs = (
        P("replica", "space", None, None),
        P("replica", "space", None, None),
        P("space", None),
        P("replica", None, "space", None),
        P("replica", None, "space", None),
        P(),
    )
    out_specs = (
        P("replica", "space", None, None),
        P("replica", None, "space", None),
        P("replica", None, "space", None),
    )
    return jax.shard_map(shards, mesh=mesh, in_specs=in_specs, out_specs=out_specs, check_vma=False)
```

```python
from functools import partial
import math

import jax
import jax.numpy as jnp
from jax import lax
from jax.sharding import PartitionSpec as P


def extended_2(shard, sides, width):
    for axis, dim in sides:
        size, length = (lax.axis_size(axis), shard.shape[dim])
        up = [(i, (i + 1) % size) for i in range(size - 1)]
        down = [(j, i) for i, j in up]
        last = lax.slice_in_dim(shard, length - width, length, axis=dim)
        initial = lax.slice_in_dim(shard, 0, width, axis=dim)
        before = lax.ppermute(last, axis, up)
        after = lax.ppermute(initial, axis, down)
        shard = jnp.concatenate([before, shard, after], axis=dim)
    return shard


def as_sent(shard):

    def short(part):
        return part.astype(jnp.bfloat16) if part.dtype == jnp.float32 else part

    return jax.tree.map(short, shard)


def passed_along(shard, axis, by):
    length = lax.axis_size(axis)
    return lax.ppermute(shard, axis, [(i, (i + by) % length) for i in range(length)])


def conv_ahead(extended, kernel):
    chan_count = extended.shape[-1]
    taps = kernel.reshape(3, 3, chan_count, kernel.shape[1])
    return lax.conv_general_dilated(
        extended[None],
        taps,
        (1, 1),
        ((0, 0), (1, 1)),
        dimension_numbers=("NHWC", "HWIO", "NHWC"),
        preferred_element_type=jnp.float32,
    )[0]


def conv_behind(extended, kernel):
    chan_count = kernel.shape[0] // 9
    taps = jnp.flip(kernel.reshape(3, 3, chan_count, kernel.shape[1]), (0, 1))
    return lax.conv_general_dilated(
        extended[None],
        taps,
        (1, 1),
        ((0, 0), (1, 1)),
        dimension_numbers=("NHWC", "HWOI", "NHWC"),
        preferred_element_type=jnp.float32,
    )[0]


def kernel_grad(extended, upstream):
    grad = lax.conv_general_dilated(
        extended[None],
        upstream[None],
        (1, 1),
        ((0, 0), (1, 1)),
        dimension_numbers=("CHWN", "IHWO", "HWNC"),
        preferred_element_type=jnp.float32,
    )
    return grad.reshape(-1, grad.shape[-1])


def kernel_grad_behind(extended_upstream, field):
    grad = lax.conv_general_dilated(
        extended_upstream[None],
        field[None],
        (1, 1),
        ((0, 0), (1, 1)),
        dimension_numbers=("CHWN", "IHWO", "HWCN"),
        preferred_element_type=jnp.float32,
    )
    grad = jnp.flip(grad, (0, 1))
    return grad.reshape(-1, grad.shape[-1])


def silu_slope(preact):
    sigma = jax.nn.sigmoid(preact)
    return sigma * (1.0 + preact * (1.0 - sigma))


def rim(stacked):
    return extended_2(stacked, (("space", 1),), 1)


def send_both(distance, stacked):
    return jax.tree.map(
        lambda part, own: part.astype(own.dtype),
        passed_along(as_sent(stacked), "replica", distance),
        stacked,
    )


def gossip(step, stacked, sender):
    levels = lax.axis_size("replica").bit_length() - 1
    received = lax.switch(
        step[0] % levels, [partial(sender, 1 << power) for power in range(levels)], stacked
    )
    return 0.5 * (stacked + received)


def swapped(part, bit):
    count = lax.axis_size("space")
    return lax.ppermute(part, "space", [(i, i ^ (1 << bit)) for i in range(count)])


def space_bits():
    return lax.axis_size("space").bit_length() - 1


def gathered_kernels(weights):
    count = lax.axis_size("space")
    own = weights[0].astype(jnp.bfloat16)
    copies = jnp.broadcast_to(own[None], (count,) + own.shape)
    have = lax.all_to_all(copies, "space", 0, 0, tiled=True)
    kernels = jnp.moveaxis(have, 0, 1)
    return kernels.reshape(kernels.shape[0], -1, kernels.shape[-1])


def scattered(grad):
    count = lax.axis_size("space")
    blocks = grad.reshape((grad.shape[0], count, -1) + grad.shape[2:])
    received = lax.all_to_all(
        jnp.moveaxis(blocks, 1, 0).astype(jnp.bfloat16), "space", 0, 0, tiled=True
    )
    return jnp.sum(received.astype(jnp.float32), axis=0)


def shards(inputs, cotangent, land_mask, weights, momentum, step):
    row_count = inputs.shape[1]
    col_count = inputs.shape[2]
    space_count = lax.axis_size("space")
    scale = 1.0 / math.sqrt(row_count * space_count * col_count)
    masked = cotangent[0] * land_mask.astype(jnp.bfloat16)[:, :, None]
    kernels = gathered_kernels(weights)
    kernel_first = kernels[0]
    kernel_second = kernels[1]
    paired = rim(jnp.stack([inputs[0], masked]))
    input_ext = paired[0]
    masked_ext = paired[1]
    preact = conv_ahead(input_ext, kernel_first)
    hidden = jax.nn.silu(preact).astype(jnp.bfloat16)
    grad_second = kernel_grad_behind(masked_ext, hidden) * scale
    back_mid = (conv_behind(masked_ext, kernel_second) * silu_slope(preact)).astype(jnp.bfloat16)
    grad_first = kernel_grad(input_ext, back_mid) * scale
    back_ext = rim(back_mid[None])[0]
    grad_input = (conv_behind(back_ext, kernel_first) + masked.astype(jnp.float32)).astype(
        jnp.bfloat16
    )[None]
    shares = scattered(jnp.stack([grad_first, grad_second]))[None]
    moment = 0.9 * momentum + shares
    updated = weights - 0.01 * moment
    mixed = gossip(step, jnp.stack([updated, moment]), send_both)
    new_weights = mixed[0]
    new_momentum = mixed[1]
    return (grad_input, new_weights, new_momentum)


def solution(mesh):
    in_specs = (
        P("replica", "space", None, None),
        P("replica", "space", None, None),
        P("space", None),
        P("replica", None, "space", None),
        P("replica", None, "space", None),
        P(),
    )
    out_specs = (
        P("replica", "space", None, None),
        P("replica", None, "space", None),
        P("replica", None, "space", None),
    )
    return jax.shard_map(shards, mesh=mesh, in_specs=in_specs, out_specs=out_specs, check_vma=False)
```

```python
from functools import partial
import math

import jax
import jax.numpy as jnp
from jax import lax
from jax.sharding import PartitionSpec as P


def extended_2(shard, sides, width):
    for axis, dim in sides:
        size, length = (lax.axis_size(axis), shard.shape[dim])
        up = [(i, (i + 1) % size) for i in range(size - 1)]
        down = [(j, i) for i, j in up]
        last = lax.slice_in_dim(shard, length - width, length, axis=dim)
        initial = lax.slice_in_dim(shard, 0, width, axis=dim)
        before = lax.ppermute(last, axis, up)
        after = lax.ppermute(initial, axis, down)
        shard = jnp.concatenate([before, shard, after], axis=dim)
    return shard


def as_sent(shard):

    def short(part):
        return part.astype(jnp.bfloat16) if part.dtype == jnp.float32 else part

    return jax.tree.map(short, shard)


def passed_along(shard, axis, by):
    length = lax.axis_size(axis)
    return lax.ppermute(shard, axis, [(i, (i + by) % length) for i in range(length)])


def conv_ahead(extended, kernel):
    chan_count = extended.shape[-1]
    taps = kernel.reshape(3, 3, chan_count, kernel.shape[1])
    return lax.conv_general_dilated(
        extended[None],
        taps,
        (1, 1),
        ((0, 0), (1, 1)),
        dimension_numbers=("NHWC", "HWIO", "NHWC"),
        preferred_element_type=jnp.float32,
    )[0]


def conv_behind(extended, kernel):
    chan_count = kernel.shape[0] // 9
    taps = jnp.flip(kernel.reshape(3, 3, chan_count, kernel.shape[1]), (0, 1))
    return lax.conv_general_dilated(
        extended[None],
        taps,
        (1, 1),
        ((0, 0), (1, 1)),
        dimension_numbers=("NHWC", "HWOI", "NHWC"),
        preferred_element_type=jnp.float32,
    )[0]


def kernel_grad(extended, upstream):
    grad = lax.conv_general_dilated(
        extended[None],
        upstream[None],
        (1, 1),
        ((0, 0), (1, 1)),
        dimension_numbers=("CHWN", "IHWO", "HWNC"),
        preferred_element_type=jnp.float32,
    )
    return grad.reshape(-1, grad.shape[-1])


def kernel_grad_behind(extended_upstream, field):
    grad = lax.conv_general_dilated(
        extended_upstream[None],
        field[None],
        (1, 1),
        ((0, 0), (1, 1)),
        dimension_numbers=("CHWN", "IHWO", "HWCN"),
        preferred_element_type=jnp.float32,
    )
    grad = jnp.flip(grad, (0, 1))
    return grad.reshape(-1, grad.shape[-1])


def silu_slope(preact):
    sigma = jax.nn.sigmoid(preact)
    return sigma * (1.0 + preact * (1.0 - sigma))


def rim(stacked):
    return extended_2(stacked, (("space", 1),), 1)


def send_both(distance, stacked):
    return jax.tree.map(
        lambda part, own: part.astype(own.dtype),
        passed_along(as_sent(stacked), "replica", distance),
        stacked,
    )


def gossip(step, stacked, sender):
    levels = lax.axis_size("replica").bit_length() - 1
    received = [sender(1 << power, stacked) for power in range(levels)]
    level = step[0] % levels
    picked = received[0]
    for power in range(1, levels):
        picked = jnp.where(level == power, received[power], picked)
    return 0.5 * (stacked + picked)


def swapped(part, bit):
    count = lax.axis_size("space")
    return lax.ppermute(part, "space", [(i, i ^ (1 << bit)) for i in range(count)])


def space_bits():
    return lax.axis_size("space").bit_length() - 1


def gathered_kernels(weights):
    count = lax.axis_size("space")
    own = weights[0].astype(jnp.bfloat16)
    copies = jnp.broadcast_to(own[None], (count,) + own.shape)
    have = lax.all_to_all(copies, "space", 0, 0, tiled=True)
    kernels = jnp.moveaxis(have, 0, 1)
    return kernels.reshape(kernels.shape[0], -1, kernels.shape[-1])


def scattered(grad):
    count = lax.axis_size("space")
    blocks = grad.reshape((grad.shape[0], count, -1) + grad.shape[2:])
    received = lax.all_to_all(
        jnp.moveaxis(blocks, 1, 0).astype(jnp.bfloat16), "space", 0, 0, tiled=True
    )
    return jnp.sum(received.astype(jnp.float32), axis=0)


def shards(inputs, cotangent, land_mask, weights, momentum, step):
    row_count = inputs.shape[1]
    col_count = inputs.shape[2]
    space_count = lax.axis_size("space")
    scale = 1.0 / math.sqrt(row_count * space_count * col_count)
    masked = cotangent[0] * land_mask.astype(jnp.bfloat16)[:, :, None]
    kernels = gathered_kernels(weights)
    kernel_first = kernels[0]
    kernel_second = kernels[1]
    paired = rim(jnp.stack([inputs[0], masked]))
    input_ext = paired[0]
    masked_ext = paired[1]
    preact = conv_ahead(input_ext, kernel_first)
    hidden = jax.nn.silu(preact).astype(jnp.bfloat16)
    grad_second = kernel_grad_behind(masked_ext, hidden) * scale
    back_mid = (conv_behind(masked_ext, kernel_second) * silu_slope(preact)).astype(jnp.bfloat16)
    grad_first = kernel_grad(input_ext, back_mid) * scale
    back_ext, grad_first, grad_second = lax.optimization_barrier(
        (rim(back_mid[None])[0], grad_first, grad_second)
    )
    grad_input = (conv_behind(back_ext, kernel_first) + masked.astype(jnp.float32)).astype(
        jnp.bfloat16
    )[None]
    shares = scattered(jnp.stack([grad_first, grad_second]))[None]
    moment = 0.9 * momentum + shares
    updated = weights - 0.01 * moment
    mixed = gossip(step, jnp.stack([updated, moment]), send_both)
    new_weights = mixed[0]
    new_momentum = mixed[1]
    return (grad_input, new_weights, new_momentum)


def solution(mesh):
    in_specs = (
        P("replica", "space", None, None),
        P("replica", "space", None, None),
        P("space", None),
        P("replica", None, "space", None),
        P("replica", None, "space", None),
        P(),
    )
    out_specs = (
        P("replica", "space", None, None),
        P("replica", None, "space", None),
        P("replica", None, "space", None),
    )
    return jax.shard_map(shards, mesh=mesh, in_specs=in_specs, out_specs=out_specs, check_vma=False)
```

```python
from functools import partial
import math

import jax
import jax.numpy as jnp
from jax import lax
from jax.sharding import PartitionSpec as P


def extended_2(shard, sides, width):
    for axis, dim in sides:
        size, length = (lax.axis_size(axis), shard.shape[dim])
        up = [(i, (i + 1) % size) for i in range(size - 1)]
        down = [(j, i) for i, j in up]
        last = lax.slice_in_dim(shard, length - width, length, axis=dim)
        initial = lax.slice_in_dim(shard, 0, width, axis=dim)
        before = lax.ppermute(last, axis, up)
        after = lax.ppermute(initial, axis, down)
        shard = jnp.concatenate([before, shard, after], axis=dim)
    return shard


def as_sent(shard):

    def short(part):
        return part.astype(jnp.bfloat16) if part.dtype == jnp.float32 else part

    return jax.tree.map(short, shard)


def passed_along(shard, axis, by):
    length = lax.axis_size(axis)
    return lax.ppermute(shard, axis, [(i, (i + by) % length) for i in range(length)])


def conv_ahead(extended, kernel):
    chan_count = extended.shape[-1]
    taps = kernel.reshape(3, 3, chan_count, kernel.shape[1])
    return lax.conv_general_dilated(
        extended[None],
        taps,
        (1, 1),
        ((0, 0), (1, 1)),
        dimension_numbers=("NHWC", "HWIO", "NHWC"),
        preferred_element_type=jnp.float32,
    )[0]


def conv_behind(extended, kernel):
    chan_count = kernel.shape[0] // 9
    taps = jnp.flip(kernel.reshape(3, 3, chan_count, kernel.shape[1]), (0, 1))
    return lax.conv_general_dilated(
        extended[None],
        taps,
        (1, 1),
        ((0, 0), (1, 1)),
        dimension_numbers=("NHWC", "HWOI", "NHWC"),
        preferred_element_type=jnp.float32,
    )[0]


def kernel_grad(extended, upstream):
    grad = lax.conv_general_dilated(
        extended[None],
        upstream[None],
        (1, 1),
        ((0, 0), (1, 1)),
        dimension_numbers=("CHWN", "IHWO", "HWNC"),
        preferred_element_type=jnp.float32,
    )
    return grad.reshape(-1, grad.shape[-1])


def kernel_grad_behind(extended_upstream, field):
    grad = lax.conv_general_dilated(
        extended_upstream[None],
        field[None],
        (1, 1),
        ((0, 0), (1, 1)),
        dimension_numbers=("CHWN", "IHWO", "HWCN"),
        preferred_element_type=jnp.float32,
    )
    grad = jnp.flip(grad, (0, 1))
    return grad.reshape(-1, grad.shape[-1])


def silu_slope(preact):
    sigma = jax.nn.sigmoid(preact)
    return sigma * (1.0 + preact * (1.0 - sigma))


def rim(stacked):
    return extended_2(stacked, (("space", 1),), 1)


def send_both(distance, stacked):
    return jax.tree.map(
        lambda part, own: part.astype(own.dtype),
        passed_along(as_sent(stacked), "replica", distance),
        stacked,
    )


def gossip(step, stacked, sender):
    levels = lax.axis_size("replica").bit_length() - 1
    received = lax.switch(
        step[0] % levels, [partial(sender, 1 << power) for power in range(levels)], stacked
    )
    return 0.5 * (stacked + received)


def swapped(part, bit):
    count = lax.axis_size("space")
    return lax.ppermute(part, "space", [(i, i ^ (1 << bit)) for i in range(count)])


def space_bits():
    return lax.axis_size("space").bit_length() - 1


def gathered_kernels(weights):
    count = lax.axis_size("space")
    own = weights[0].astype(jnp.bfloat16)
    copies = jnp.broadcast_to(own[None], (count,) + own.shape)
    have = lax.all_to_all(copies, "space", 0, 0, tiled=True)
    kernels = jnp.moveaxis(have, 0, 1)
    return kernels.reshape(kernels.shape[0], -1, kernels.shape[-1])


def scattered(grad):
    count = lax.axis_size("space")
    blocks = grad.reshape((grad.shape[0], count, -1) + grad.shape[2:])
    received = lax.all_to_all(
        jnp.moveaxis(blocks, 1, 0).astype(jnp.bfloat16), "space", 0, 0, tiled=True
    )
    return jnp.sum(received.astype(jnp.float32), axis=0)


def shards(inputs, cotangent, land_mask, weights, momentum, step):
    row_count = inputs.shape[1]
    col_count = inputs.shape[2]
    space_count = lax.axis_size("space")
    scale = 1.0 / math.sqrt(row_count * space_count * col_count)
    masked = cotangent[0] * land_mask.astype(jnp.bfloat16)[:, :, None]
    kernels = gathered_kernels(weights)
    kernel_first = kernels[0]
    kernel_second = kernels[1]
    input_ext = rim(inputs)[0]
    masked_ext = rim(masked[None])[0]
    preact = conv_ahead(input_ext, kernel_first)
    hidden = jax.nn.silu(preact).astype(jnp.bfloat16)
    grad_second = kernel_grad_behind(masked_ext, hidden) * scale
    back_mid = (conv_behind(masked_ext, kernel_second) * silu_slope(preact)).astype(jnp.bfloat16)
    grad_first = kernel_grad(input_ext, back_mid) * scale
    back_ext, grad_first, grad_second = lax.optimization_barrier(
        (rim(back_mid[None])[0], grad_first, grad_second)
    )
    grad_input = (conv_behind(back_ext, kernel_first) + masked.astype(jnp.float32)).astype(
        jnp.bfloat16
    )[None]
    shares = scattered(jnp.stack([grad_first, grad_second]))[None]
    moment = 0.9 * momentum + shares
    updated = weights - 0.01 * moment
    mixed = gossip(step, jnp.stack([updated, moment]), send_both)
    new_weights = mixed[0]
    new_momentum = mixed[1]
    return (grad_input, new_weights, new_momentum)


def solution(mesh):
    in_specs = (
        P("replica", "space", None, None),
        P("replica", "space", None, None),
        P("space", None),
        P("replica", None, "space", None),
        P("replica", None, "space", None),
        P(),
    )
    out_specs = (
        P("replica", "space", None, None),
        P("replica", None, "space", None),
        P("replica", None, "space", None),
    )
    return jax.shard_map(shards, mesh=mesh, in_specs=in_specs, out_specs=out_specs, check_vma=False)
```

```python
from functools import partial
import math

import jax
import jax.numpy as jnp
from jax import lax
from jax.sharding import PartitionSpec as P


def extended_2(shard, sides, width):
    for axis, dim in sides:
        size, length = (lax.axis_size(axis), shard.shape[dim])
        up = [(i, (i + 1) % size) for i in range(size - 1)]
        down = [(j, i) for i, j in up]
        last = lax.slice_in_dim(shard, length - width, length, axis=dim)
        initial = lax.slice_in_dim(shard, 0, width, axis=dim)
        before = lax.ppermute(last, axis, up)
        after = lax.ppermute(initial, axis, down)
        shard = jnp.concatenate([before, shard, after], axis=dim)
    return shard


def as_sent(shard):

    def short(part):
        return part.astype(jnp.bfloat16) if part.dtype == jnp.float32 else part

    return jax.tree.map(short, shard)


def passed_along(shard, axis, by):
    length = lax.axis_size(axis)
    return lax.ppermute(shard, axis, [(i, (i + by) % length) for i in range(length)])


def conv_ahead(extended, kernel):
    chan_count = extended.shape[-1]
    taps = kernel.reshape(3, 3, chan_count, kernel.shape[1])
    return lax.conv_general_dilated(
        extended[None],
        taps,
        (1, 1),
        ((0, 0), (1, 1)),
        dimension_numbers=("NHWC", "HWIO", "NHWC"),
        preferred_element_type=jnp.float32,
    )[0]


def conv_behind(extended, kernel):
    chan_count = kernel.shape[0] // 9
    taps = jnp.flip(kernel.reshape(3, 3, chan_count, kernel.shape[1]), (0, 1))
    return lax.conv_general_dilated(
        extended[None],
        taps,
        (1, 1),
        ((0, 0), (1, 1)),
        dimension_numbers=("NHWC", "HWOI", "NHWC"),
        preferred_element_type=jnp.float32,
    )[0]


def kernel_grad(extended, upstream):
    grad = lax.conv_general_dilated(
        extended[None],
        upstream[None],
        (1, 1),
        ((0, 0), (1, 1)),
        dimension_numbers=("CHWN", "IHWO", "HWNC"),
        preferred_element_type=jnp.float32,
    )
    return grad.reshape(-1, grad.shape[-1])


def kernel_grad_behind(extended_upstream, field):
    grad = lax.conv_general_dilated(
        extended_upstream[None],
        field[None],
        (1, 1),
        ((0, 0), (1, 1)),
        dimension_numbers=("CHWN", "IHWO", "HWCN"),
        preferred_element_type=jnp.float32,
    )
    grad = jnp.flip(grad, (0, 1))
    return grad.reshape(-1, grad.shape[-1])


def silu_slope(preact):
    sigma = jax.nn.sigmoid(preact)
    return sigma * (1.0 + preact * (1.0 - sigma))


def rim(stacked):
    return extended_2(stacked, (("space", 1),), 1)


def send_both(distance, stacked):
    return jax.tree.map(
        lambda part, own: part.astype(own.dtype),
        passed_along(as_sent(stacked), "replica", distance),
        stacked,
    )


def gossip(step, stacked, sender):
    levels = lax.axis_size("replica").bit_length() - 1
    received = lax.switch(
        step[0] % levels, [partial(sender, 1 << power) for power in range(levels)], stacked
    )
    return 0.5 * (stacked + received)


def swapped(part, bit):
    count = lax.axis_size("space")
    return lax.ppermute(part, "space", [(i, i ^ (1 << bit)) for i in range(count)])


def space_bits():
    return lax.axis_size("space").bit_length() - 1


def gathered_kernels(weights):
    count = lax.axis_size("space")
    own = weights[0].astype(jnp.bfloat16)
    copies = jnp.broadcast_to(own[None], (count,) + own.shape)
    have = lax.all_to_all(copies, "space", 0, 0, tiled=True)
    kernels = jnp.moveaxis(have, 0, 1)
    return kernels.reshape(kernels.shape[0], -1, kernels.shape[-1])


def scattered(grad):
    count = lax.axis_size("space")
    blocks = grad.reshape((grad.shape[0], count, -1) + grad.shape[2:])
    received = lax.all_to_all(
        jnp.moveaxis(blocks, 1, 0).astype(jnp.bfloat16), "space", 0, 0, tiled=True
    )
    return jnp.sum(received.astype(jnp.float32), axis=0)


def shards(inputs, cotangent, land_mask, weights, momentum, step):
    row_count = inputs.shape[1]
    col_count = inputs.shape[2]
    space_count = lax.axis_size("space")
    scale = 1.0 / math.sqrt(row_count * space_count * col_count)
    masked = cotangent[0] * land_mask.astype(jnp.bfloat16)[:, :, None]
    kernels = gathered_kernels(weights)
    kernel_first = kernels[0]
    kernel_second = kernels[1]
    paired = rim(jnp.stack([inputs[0], masked]))
    input_ext = paired[0]
    masked_ext = paired[1]
    preact = conv_ahead(input_ext, kernel_first)
    hidden = jax.nn.silu(preact).astype(jnp.bfloat16)
    grad_second = kernel_grad_behind(masked_ext, hidden) * scale
    back_mid = (conv_behind(masked_ext, kernel_second) * silu_slope(preact)).astype(jnp.bfloat16)
    back_ext = rim(back_mid[None])[0]
    grad_first = kernel_grad_behind(back_ext, inputs[0]) * scale
    grad_input = (conv_behind(back_ext, kernel_first) + masked.astype(jnp.float32)).astype(
        jnp.bfloat16
    )[None]
    shares = scattered(jnp.stack([grad_first, grad_second]))[None]
    moment = 0.9 * momentum + shares
    updated = weights - 0.01 * moment
    mixed = gossip(step, jnp.stack([updated, moment]), send_both)
    new_weights = mixed[0]
    new_momentum = mixed[1]
    return (grad_input, new_weights, new_momentum)


def solution(mesh):
    in_specs = (
        P("replica", "space", None, None),
        P("replica", "space", None, None),
        P("space", None),
        P("replica", None, "space", None),
        P("replica", None, "space", None),
        P(),
    )
    out_specs = (
        P("replica", "space", None, None),
        P("replica", None, "space", None),
        P("replica", None, "space", None),
    )
    return jax.shard_map(shards, mesh=mesh, in_specs=in_specs, out_specs=out_specs, check_vma=False)
```
